128 devices in a mesh: dp: 16 (over z, x), tensor: 8 (over y, core).
Axes of the slice: x: 4, y: 4, z: 4, core: 2. Of those that a mesh axis runs over, the one named last changes fastest.
Arguments:
- tokens: bfloat16 [8192, 8192], P('dp', 'tensor'), may hold values from -6 to 6
- cotangent: bfloat16 [8192, 4096], P('dp', 'tensor'), may hold values from -1.5 to 1.5
- frozen_query_weight: bfloat16 [8192, 4096], P(None, 'tensor'), may hold values from -0.0625 to 0.0625
- adapter_down_weight: bfloat16 [256, 8192, 64], P('dp', 'tensor'), may hold values from -0.0625 to 0.0625
- adapter_up_weight: bfloat16 [256, 64, 4096], P('dp', None, 'tensor'), may hold values from -0.75 to 0.75
- token_adapter: int32 [8192], P('dp'), may hold values from 0 to 255, as said below
Outputs:
- projected: bfloat16 [8192, 4096], P('dp', 'tensor')
- input_gradient: bfloat16 [8192, 8192], P('dp', 'tensor')
- down_grad: float32 [256, 8192, 64], P('dp', 'tensor')
- up_grad: float32 [256, 64, 4096], P('dp', None, 'tensor')
The draws below stay inside these ranges and needn't reach their ends.
Inputs may be any that keep to these rules, and one draw needn't show every extreme that they name: `token_adapter`: adapter a belongs to index a // 16 of dp. Among the 512 tokens of one index of dp, at most 64 have adapters that belong to one index of dp, and for some index exactly 64 do.
All inputs are finite; a program needn't handle non-finite values.
Results may differ from the reference program's by a relative error of at most 0.0037.
Values may be sent and summed in bfloat16 or wider, within the bound.
No kernel may reach another device: no remote copies, remote signals or barrier semaphores. Data moves between devices by JAX's collectives and lax.ppermute only.
A program may use at most 192 MiB of HBM per device.

```python
import math
import jax
import jax.numpy as jnp
from jax import lax

MODEL_WIDTH = 8192
ADAPTER_RANK = 64
AD_DEV = 16
TOK_DEV = 512
QUERY_FEATURES = 4096
ADAPTER_TOTAL = 256
CAP = 64
TOKEN_TOTAL = 8192


def draw_token_adapter(key, part):
    owner_count = TOKEN_TOTAL // TOK_DEV

    def one_block(block_key):
        key_hot, key_rest, key_order, key_local = jax.random.split(block_key, 4)
        hot_owner = jax.random.randint(key_hot, (), 0, owner_count)
        shifts = jnp.repeat(jnp.arange(owner_count - 1), CAP)
        others = (hot_owner + 1 + shifts) % owner_count
        others = jax.random.permutation(key_rest, others)[:TOK_DEV - CAP]
        owner_list = jnp.concatenate([jnp.full((CAP,), hot_owner), others])
        owner_list = jax.random.permutation(key_order, owner_list)
        local_pick = jax.random.randint(key_local, (TOK_DEV,), 0, AD_DEV)
        return (owner_list * AD_DEV + local_pick).astype(jnp.int32)
    block_keys = jax.random.split(key, owner_count)
    return jax.vmap(one_block)(block_keys).reshape(TOKEN_TOTAL).astype(jnp.int32)


def block_scale(key, dims, cuts, low, high):
    level = 1.0
    for axis_at, shards_of in cuts:
        steps = jax.random.uniform(jax.random.fold_in(jax.random.fold_in(key, 6), axis_at), (shards_of,), jnp.float32, low / len(cuts), high / len(cuts))
        level = level * jnp.repeat(jnp.exp(steps), dims[axis_at] // shards_of).reshape((-1,) + (1,) * (len(dims) - 1 - axis_at))
    return level


def normal_values(rng, shape, spread, bound, cuts=(), held_as=jnp.bfloat16):
    gain = block_scale(rng, shape, cuts, -0.22, 0.18) if cuts else 1.0
    values = jax.random.normal(rng, shape, jnp.float32) * spread * gain
    return jnp.minimum(jnp.maximum(values, -bound), bound).astype(held_as)


def setup_inputs(seed: int = 0) -> dict:
    splits = jax.random.split(jax.random.key(seed), 7)
    return {
        "tokens": normal_values(splits[0], (TOKEN_TOTAL, MODEL_WIDTH), 1.0, 6.0, ((0, 16), (1, 8))),
        "cotangent": normal_values(splits[1], (TOKEN_TOTAL, QUERY_FEATURES), 0.25, 1.5, ((0, 16), (1, 8))),
        "frozen_query_weight": normal_values(splits[2], (MODEL_WIDTH, QUERY_FEATURES), MODEL_WIDTH ** -0.5, 0.0625, ((1, 8),)),
        "adapter_down_weight": normal_values(splits[3], (ADAPTER_TOTAL, MODEL_WIDTH, ADAPTER_RANK), MODEL_WIDTH ** -0.5, 0.0625, ((0, 16), (1, 8))),
        "adapter_up_weight": normal_values(splits[4], (ADAPTER_TOTAL, ADAPTER_RANK, QUERY_FEATURES), ADAPTER_RANK ** -0.5, 0.75, ((0, 16), (2, 8))),
        "token_adapter": draw_token_adapter(jax.random.fold_in(splits[6], 71), 0),
    }


adapter_factor = 0.5


def reference(tokens, cotangent, frozen_query_weight, adapter_down_weight, adapter_up_weight, token_adapter):
    frozen_output = jnp.dot(tokens, frozen_query_weight, preferred_element_type=jnp.float32)
    frozen_backward = jnp.dot(cotangent, frozen_query_weight.T, preferred_element_type=jnp.float32)
    block_rows = math.gcd(TOKEN_TOTAL, 64)
    block_count = TOKEN_TOTAL // block_rows
    token_blocks = tokens.reshape(block_count, block_rows, MODEL_WIDTH)
    grad_blocks = cotangent.reshape(block_count, block_rows, QUERY_FEATURES)
    id_blocks = token_adapter.reshape(block_count, block_rows).astype(jnp.int32)

    def one_block(grads, inputs):
        down_running_sum, up_running_sum = grads
        block_tokens, block_cot, block_numbers = inputs
        down_weight_rows = adapter_down_weight[block_numbers].astype(jnp.float32)
        up_weight_rows = adapter_up_weight[block_numbers].astype(jnp.float32)
        tokens_wide = block_tokens.astype(jnp.float32)
        cot_wide = block_cot.astype(jnp.float32)
        low_hidden = jnp.einsum('nd,ndr->nr', tokens_wide, down_weight_rows)
        lowrank_round = low_hidden.astype(jnp.bfloat16)
        low_grad = jnp.einsum('nq,nrq->nr', cot_wide, up_weight_rows)
        gradient_round = (adapter_factor * low_grad).astype(jnp.bfloat16)
        adapter_output = (adapter_factor * jnp.einsum('fe,fek->fk', lowrank_round.astype(jnp.float32), up_weight_rows)).astype(jnp.bfloat16)
        adapter_backward = jnp.einsum('vl,vwl->vw', gradient_round.astype(jnp.float32), down_weight_rows).astype(jnp.bfloat16)
        down_running_sum = down_running_sum.at[block_numbers].add(jnp.einsum('nd,nr->ndr', tokens_wide, gradient_round.astype(jnp.float32)))
        up_running_sum = up_running_sum.at[block_numbers].add(adapter_factor * jnp.einsum('nr,nq->nrq', lowrank_round.astype(jnp.float32), cot_wide))
        return (down_running_sum, up_running_sum), (adapter_output, adapter_backward)

    start_grads = (jnp.zeros((ADAPTER_TOTAL, MODEL_WIDTH, ADAPTER_RANK), jnp.float32), jnp.zeros((ADAPTER_TOTAL, ADAPTER_RANK, QUERY_FEATURES), jnp.float32))
    final_grads, output_rows = lax.scan(one_block, start_grads, (token_blocks, grad_blocks, id_blocks))
    adapter_output = output_rows[0].reshape(TOKEN_TOTAL, QUERY_FEATURES)
    adapter_backward = output_rows[1].reshape(TOKEN_TOTAL, MODEL_WIDTH)
    projected = (frozen_output + adapter_output.astype(jnp.float32)).astype(jnp.bfloat16)
    input_gradient = (frozen_backward + adapter_backward.astype(jnp.float32)).astype(jnp.bfloat16)
    return projected, input_gradient, final_grads[0], final_grads[1]
```

```python
import jax
import jax.numpy as jnp
from jax import lax
from jax.sharding import PartitionSpec as P

adapter_factor = 0.5


def tensor_sum(x):
    n = lax.axis_size("tensor")
    rows = x.shape[0]
    parts = x.reshape(n, rows // n, *x.shape[1:])
    got = lax.all_to_all(parts, "tensor", split_axis=0, concat_axis=0, tiled=True)
    mine = jnp.sum(got, axis=0)
    spread = jnp.broadcast_to(mine[None], (n,) + mine.shape)
    full = lax.all_to_all(spread, "tensor", split_axis=0, concat_axis=0, tiled=True)
    return full.reshape(x.shape)


def per_device(
    tokens, cotangent, frozen_query_weight, adapter_down_weight, adapter_up_weight, token_adapter
):
    tok_rows, feature_portion = tokens.shape
    query_portion = cotangent.shape[1]
    local_adapters, _, rank_columns = adapter_down_weight.shape
    dp_size = lax.axis_size("dp")
    capacity = tok_rows // dp_size * 2
    capacity = min(capacity, tok_rows)
    slot_count = dp_size * capacity
    oh_width = 128

    tokens_full = lax.all_gather(tokens, "tensor", axis=1, tiled=True)
    partial_term = lax.dot_general(
        cotangent, frozen_query_weight, (((1,), (1,)), ((), ())), preferred_element_type=jnp.float32
    )
    frozen_backward = lax.psum_scatter(partial_term, "tensor", scatter_dimension=1, tiled=True)

    owners = token_adapter // local_adapters
    local_ids = token_adapter % local_adapters
    owner_hits = (owners[:, None] == jnp.arange(dp_size, dtype=jnp.int32)[None, :]).astype(jnp.int32)
    earlier = jnp.cumsum(owner_hits, axis=0) - owner_hits
    rank_in = jnp.sum(earlier * owner_hits, axis=1)
    slot_of = owners * capacity + rank_in
    pick = (jnp.arange(slot_count, dtype=jnp.int32)[:, None] == slot_of[None, :]).astype(jnp.bfloat16)
    local_hot = (local_ids[:, None] == jnp.arange(oh_width, dtype=jnp.int32)[None, :]).astype(
        jnp.bfloat16
    )
    payload = jnp.concatenate([tokens, cotangent, local_hot], axis=1)
    send = jnp.dot(pick, payload, preferred_element_type=jnp.float32).astype(jnp.bfloat16)
    got = lax.all_to_all(send, "dp", split_axis=0, concat_axis=0, tiled=True)
    got_tok = got[:, :feature_portion]
    got_cot = got[:, feature_portion : feature_portion + query_portion]
    got_hot = got[:, feature_portion + query_portion : feature_portion + query_portion + local_adapters]
    hot_f = got_hot.astype(jnp.float32)

    hidden_all = jnp.einsum(
        "sd,adr->sar", got_tok, adapter_down_weight, preferred_element_type=jnp.float32
    )
    grad_all = jnp.einsum(
        "sq,arq->sar", got_cot, adapter_up_weight, preferred_element_type=jnp.float32
    )
    hidden_part = jnp.sum(hidden_all * hot_f[:, :, None], axis=1)
    grad_part = jnp.sum(grad_all * hot_f[:, :, None], axis=1)
    joined = tensor_sum(jnp.concatenate([hidden_part, grad_part], axis=1))
    lowrank_round = joined[:, :rank_columns].astype(jnp.bfloat16)
    gradient_round = (adapter_factor * joined[:, rank_columns:]).astype(jnp.bfloat16)
    low_spread = got_hot[:, :, None] * lowrank_round[:, None, :]
    grad_spread = got_hot[:, :, None] * gradient_round[:, None, :]

    adapter_output = (
        adapter_factor
        * jnp.einsum("sar,arq->sq", low_spread, adapter_up_weight, preferred_element_type=jnp.float32)
    ).astype(jnp.bfloat16)
    adapter_backward = jnp.einsum(
        "sar,adr->sd", grad_spread, adapter_down_weight, preferred_element_type=jnp.float32
    ).astype(jnp.bfloat16)
    down_grad = jnp.einsum("sd,sar->adr", got_tok, grad_spread, preferred_element_type=jnp.float32)
    up_grad = adapter_factor * jnp.einsum(
        "sar,sq->arq", low_spread, got_cot, preferred_element_type=jnp.float32
    )

    back = jnp.concatenate([adapter_output, adapter_backward], axis=1)
    back = lax.all_to_all(back, "dp", split_axis=0, concat_axis=0, tiled=True)
    mine = jnp.einsum("st,sc->tc", pick, back, preferred_element_type=jnp.float32)
    mine_out = mine[:, :query_portion]
    mine_grad = mine[:, query_portion:]

    frozen_output = jnp.dot(tokens_full, frozen_query_weight, preferred_element_type=jnp.float32)
    projected = (frozen_output + mine_out).astype(jnp.bfloat16)
    input_gradient = (frozen_backward + mine_grad).astype(jnp.bfloat16)
    return (projected, input_gradient, down_grad, up_grad)


def solution(mesh):
    in_specs = (
        P("dp", "tensor"),
        P("dp", "tensor"),
        P(None, "tensor"),
        P("dp", "tensor", None),
        P("dp", None, "tensor"),
        P("dp"),
    )
    out_specs = (
        P("dp", "tensor"),
        P("dp", "tensor"),
        P("dp", "tensor", None),
        P("dp", None, "tensor"),
    )
    return jax.shard_map(
        per_device, mesh=mesh, in_specs=in_specs, out_specs=out_specs, check_vma=False
    )
```

```python
import jax
import jax.numpy as jnp
from jax import lax
from jax.sharding import PartitionSpec as P

adapter_factor = 0.5


def tensor_sum(x):
    n = lax.axis_size("tensor")
    rows = x.shape[0]
    parts = x.reshape(n, rows // n, *x.shape[1:])
    got = lax.all_to_all(parts, "tensor", split_axis=0, concat_axis=0, tiled=True)
    mine = jnp.sum(got, axis=0)
    spread = jnp.broadcast_to(mine[None], (n,) + mine.shape)
    full = lax.all_to_all(spread, "tensor", split_axis=0, concat_axis=0, tiled=True)
    return full.reshape(x.shape)


def per_device(
    tokens, cotangent, frozen_query_weight, adapter_down_weight, adapter_up_weight, token_adapter
):
    tok_rows, feature_portion = tokens.shape
    query_portion = cotangent.shape[1]
    local_adapters, _, rank_columns = adapter_down_weight.shape
    dp_size = lax.axis_size("dp")
    capacity = tok_rows // dp_size * 2
    capacity = min(capacity, tok_rows)
    slot_count = dp_size * capacity
    oh_width = 128

    tokens_full = lax.all_gather(tokens, "tensor", axis=1, tiled=True)

    owners = token_adapter // local_adapters
    local_ids = token_adapter % local_adapters
    owner_hits = (owners[:, None] == jnp.arange(dp_size, dtype=jnp.int32)[None, :]).astype(jnp.int32)
    earlier = jnp.cumsum(owner_hits, axis=0) - owner_hits
    rank_in = jnp.sum(earlier * owner_hits, axis=1)
    slot_of = owners * capacity + rank_in
    pick = (jnp.arange(slot_count, dtype=jnp.int32)[:, None] == slot_of[None, :]).astype(jnp.bfloat16)
    local_hot = (local_ids[:, None] == jnp.arange(oh_width, dtype=jnp.int32)[None, :]).astype(
        jnp.bfloat16
    )
    payload = jnp.concatenate([tokens, cotangent, local_hot], axis=1)
    send = jnp.dot(pick, payload, preferred_element_type=jnp.float32).astype(jnp.bfloat16)
    send, cot_late, weight_late = lax.optimization_barrier((send, cotangent, frozen_query_weight))
    partial_term = lax.dot_general(
        cot_late, weight_late, (((1,), (1,)), ((), ())), preferred_element_type=jnp.float32
    )
    frozen_backward = lax.psum_scatter(partial_term, "tensor", scatter_dimension=1, tiled=True)
    got = lax.all_to_all(send, "dp", split_axis=0, concat_axis=0, tiled=True)
    got_tok = got[:, :feature_portion]
    got_cot = got[:, feature_portion : feature_portion + query_portion]
    got_hot = got[:, feature_portion + query_portion : feature_portion + query_portion + local_adapters]
    hot_f = got_hot.astype(jnp.float32)

    hidden_all = jnp.einsum(
        "sd,adr->sar", got_tok, adapter_down_weight, preferred_element_type=jnp.float32
    )
    grad_all = jnp.einsum(
        "sq,arq->sar", got_cot, adapter_up_weight, preferred_element_type=jnp.float32
    )
    hidden_part = jnp.sum(hidden_all * hot_f[:, :, None], axis=1)
    grad_part = jnp.sum(grad_all * hot_f[:, :, None], axis=1)
    joined = tensor_sum(jnp.concatenate([hidden_part, grad_part], axis=1))
    lowrank_round = joined[:, :rank_columns].astype(jnp.bfloat16)
    gradient_round = (adapter_factor * joined[:, rank_columns:]).astype(jnp.bfloat16)
    low_spread = got_hot[:, :, None] * lowrank_round[:, None, :]
    grad_spread = got_hot[:, :, None] * gradient_round[:, None, :]

    adapter_output = (
        adapter_factor
        * jnp.einsum("sar,arq->sq", low_spread, adapter_up_weight, preferred_element_type=jnp.float32)
    ).astype(jnp.bfloat16)
    adapter_backward = jnp.einsum(
        "sar,adr->sd", grad_spread, adapter_down_weight, preferred_element_type=jnp.float32
    ).astype(jnp.bfloat16)
    down_grad = jnp.einsum("sd,sar->adr", got_tok, grad_spread, preferred_element_type=jnp.float32)
    up_grad = adapter_factor * jnp.einsum(
        "sar,sq->arq", low_spread, got_cot, preferred_element_type=jnp.float32
    )

    back = jnp.concatenate([adapter_output, adapter_backward], axis=1)
    back, tokens_late = lax.optimization_barrier((back, tokens_full))
    back = lax.all_to_all(back, "dp", split_axis=0, concat_axis=0, tiled=True)
    frozen_output = lax.optimization_barrier(
        jnp.dot(tokens_late, frozen_query_weight, preferred_element_type=jnp.float32)
    )
    mine = jnp.einsum("st,sc->tc", pick, back, preferred_element_type=jnp.float32)
    mine_out = mine[:, :query_portion]
    mine_grad = mine[:, query_portion:]

    projected = (frozen_output + mine_out).astype(jnp.bfloat16)
    input_gradient = (frozen_backward + mine_grad).astype(jnp.bfloat16)
    return (projected, input_gradient, down_grad, up_grad)


def solution(mesh):
    in_specs = (
        P("dp", "tensor"),
        P("dp", "tensor"),
        P(None, "tensor"),
        P("dp", "tensor", None),
        P("dp", None, "tensor"),
        P("dp"),
    )
    out_specs = (
        P("dp", "tensor"),
        P("dp", "tensor"),
        P("dp", "tensor", None),
        P("dp", None, "tensor"),
    )
    return jax.shard_map(
        per_device, mesh=mesh, in_specs=in_specs, out_specs=out_specs, check_vma=False
    )
```

```python
import jax
import jax.numpy as jnp
from jax import lax
from jax.sharding import PartitionSpec as P

adapter_factor = 0.5


def tensor_sum(x):
    n = lax.axis_size("tensor")
    step = 1
    while step < n:
        perm = [(t, t ^ step) for t in range(n)]
        x = x + lax.ppermute(x, "tensor", perm)
        step *= 2
    return x


def per_device(
    tokens, cotangent, frozen_query_weight, adapter_down_weight, adapter_up_weight, token_adapter
):
    tok_rows, feature_portion = tokens.shape
    query_portion = cotangent.shape[1]
    local_adapters, _, rank_columns = adapter_down_weight.shape
    dp_size = lax.axis_size("dp")
    capacity = tok_rows // dp_size * 2
    capacity = min(capacity, tok_rows)
    slot_count = dp_size * capacity
    oh_width = 128

    tokens_full = lax.all_gather(tokens, "tensor", axis=1, tiled=True)

    owners = token_adapter // local_adapters
    local_ids = token_adapter % local_adapters
    owner_hits = (owners[:, None] == jnp.arange(dp_size, dtype=jnp.int32)[None, :]).astype(jnp.int32)
    earlier = jnp.cumsum(owner_hits, axis=0) - owner_hits
    rank_in = jnp.sum(earlier * owner_hits, axis=1)
    slot_of = owners * capacity + rank_in
    pick = (jnp.arange(slot_count, dtype=jnp.int32)[:, None] == slot_of[None, :]).astype(jnp.bfloat16)
    local_hot = (local_ids[:, None] == jnp.arange(oh_width, dtype=jnp.int32)[None, :]).astype(
        jnp.bfloat16
    )
    payload = jnp.concatenate([tokens, cotangent, local_hot], axis=1)
    send = jnp.dot(pick, payload, preferred_element_type=jnp.float32).astype(jnp.bfloat16)
    send, cot_late, weight_late = lax.optimization_barrier((send, cotangent, frozen_query_weight))
    partial_term = lax.dot_general(
        cot_late, weight_late, (((1,), (1,)), ((), ())), preferred_element_type=jnp.float32
    )
    frozen_backward = lax.psum_scatter(partial_term, "tensor", scatter_dimension=1, tiled=True)
    got = lax.all_to_all(send, "dp", split_axis=0, concat_axis=0, tiled=True)
    got_tok = got[:, :feature_portion]
    got_cot = got[:, feature_portion : feature_portion + query_portion]
    got_hot = got[:, feature_portion + query_portion : feature_portion + query_portion + local_adapters]
    hot_f = got_hot.astype(jnp.float32)

    hidden_all = jnp.einsum(
        "sd,adr->sar", got_tok, adapter_down_weight, preferred_element_type=jnp.float32
    )
    grad_all = jnp.einsum(
        "sq,arq->sar", got_cot, adapter_up_weight, preferred_element_type=jnp.float32
    )
    hidden_part = jnp.sum(hidden_all * hot_f[:, :, None], axis=1)
    grad_part = jnp.sum(grad_all * hot_f[:, :, None], axis=1)
    joined = tensor_sum(jnp.concatenate([hidden_part, grad_part], axis=1))
    lowrank_round = joined[:, :rank_columns].astype(jnp.bfloat16)
    gradient_round = (adapter_factor * joined[:, rank_columns:]).astype(jnp.bfloat16)
    low_spread = got_hot[:, :, None] * lowrank_round[:, None, :]
    grad_spread = got_hot[:, :, None] * gradient_round[:, None, :]

    adapter_output = (
        adapter_factor
        * jnp.einsum("sar,arq->sq", low_spread, adapter_up_weight, preferred_element_type=jnp.float32)
    ).astype(jnp.bfloat16)
    adapter_backward = jnp.einsum(
        "sar,adr->sd", grad_spread, adapter_down_weight, preferred_element_type=jnp.float32
    ).astype(jnp.bfloat16)
    down_grad = jnp.einsum("sd,sar->adr", got_tok, grad_spread, preferred_element_type=jnp.float32)
    up_grad = adapter_factor * jnp.einsum(
        "sar,sq->arq", low_spread, got_cot, preferred_element_type=jnp.float32
    )

    back = jnp.concatenate([adapter_output, adapter_backward], axis=1)
    back, tokens_late = lax.optimization_barrier((back, tokens_full))
    back = lax.all_to_all(back, "dp", split_axis=0, concat_axis=0, tiled=True)
    frozen_output = lax.optimization_barrier(
        jnp.dot(tokens_late, frozen_query_weight, preferred_element_type=jnp.float32)
    )
    mine = jnp.einsum("st,sc->tc", pick, back, preferred_element_type=jnp.float32)
    mine_out = mine[:, :query_portion]
    mine_grad = mine[:, query_portion:]

    projected = (frozen_output + mine_out).astype(jnp.bfloat16)
    input_gradient = (frozen_backward + mine_grad).astype(jnp.bfloat16)
    return (projected, input_gradient, down_grad, up_grad)


def solution(mesh):
    in_specs = (
        P("dp", "tensor"),
        P("dp", "tensor"),
        P(None, "tensor"),
        P("dp", "tensor", None),
        P("dp", None, "tensor"),
        P("dp"),
    )
    out_specs = (
        P("dp", "tensor"),
        P("dp", "tensor"),
        P("dp", "tensor", None),
        P("dp", None, "tensor"),
    )
    return jax.shard_map(
        per_device, mesh=mesh, in_specs=in_specs, out_specs=out_specs, check_vma=False
    )
```

```python
import jax
import jax.numpy as jnp
from jax import lax
from jax.sharding import PartitionSpec as P

adapter_factor = 0.5


def tensor_sum(x):
    n = lax.axis_size("tensor")
    half = x.shape[0] // 2
    core = lax.axis_index("tensor") % 2
    keep = lax.dynamic_slice_in_dim(x, core * half, half, axis=0)
    give = lax.dynamic_slice_in_dim(x, (1 - core) * half, half, axis=0)
    pair = [(t, t ^ 1) for t in range(n)]
    mine = keep + lax.ppermute(give, "tensor", pair)
    step = 2
    while step < n:
        perm = [(t, t ^ step) for t in range(n)]
        mine = mine + lax.ppermute(mine, "tensor", perm)
        step *= 2
    other = lax.ppermute(mine, "tensor", pair)
    first = jnp.where(core == 0, mine, other)
    second = jnp.where(core == 0, other, mine)
    return jnp.concatenate([first, second], axis=0)


def per_device(
    tokens, cotangent, frozen_query_weight, adapter_down_weight, adapter_up_weight, token_adapter
):
    tok_rows, feature_portion = tokens.shape
    query_portion = cotangent.shape[1]
    local_adapters, _, rank_columns = adapter_down_weight.shape
    dp_size = lax.axis_size("dp")
    capacity = tok_rows // dp_size * 2
    capacity = min(capacity, tok_rows)
    slot_count = dp_size * capacity
    oh_width = 128

    tokens_full = lax.all_gather(tokens, "tensor", axis=1, tiled=True)

    owners = token_adapter // local_adapters
    local_ids = token_adapter % local_adapters
    owner_hits = (owners[:, None] == jnp.arange(dp_size, dtype=jnp.int32)[None, :]).astype(jnp.int32)
    earlier = jnp.cumsum(owner_hits, axis=0) - owner_hits
    rank_in = jnp.sum(earlier * owner_hits, axis=1)
    slot_of = owners * capacity + rank_in
    pick = (jnp.arange(slot_count, dtype=jnp.int32)[:, None] == slot_of[None, :]).astype(jnp.bfloat16)
    local_hot = (local_ids[:, None] == jnp.arange(oh_width, dtype=jnp.int32)[None, :]).astype(
        jnp.bfloat16
    )
    payload = jnp.concatenate([tokens, cotangent, local_hot], axis=1)
    send = jnp.dot(pick, payload, preferred_element_type=jnp.float32).astype(jnp.bfloat16)
    send, cot_late, weight_late = lax.optimization_barrier((send, cotangent, frozen_query_weight))
    partial_term = lax.dot_general(
        cot_late, weight_late, (((1,), (1,)), ((), ())), preferred_element_type=jnp.float32
    )
    frozen_backward = lax.psum_scatter(partial_term, "tensor", scatter_dimension=1, tiled=True)
    got = lax.all_to_all(send, "dp", split_axis=0, concat_axis=0, tiled=True)
    got_tok = got[:, :feature_portion]
    got_cot = got[:, feature_portion : feature_portion + query_portion]
    got_hot = got[:, feature_portion + query_portion : feature_portion + query_portion + local_adapters]
    hot_f = got_hot.astype(jnp.float32)

    hidden_all = jnp.einsum(
        "sd,adr->sar", got_tok, adapter_down_weight, preferred_element_type=jnp.float32
    )
    grad_all = jnp.einsum(
        "sq,arq->sar", got_cot, adapter_up_weight, preferred_element_type=jnp.float32
    )
    hidden_part = jnp.sum(hidden_all * hot_f[:, :, None], axis=1)
    grad_part = jnp.sum(grad_all * hot_f[:, :, None], axis=1)
    joined = tensor_sum(jnp.concatenate([hidden_part, grad_part], axis=1))
    lowrank_round = joined[:, :rank_columns].astype(jnp.bfloat16)
    gradient_round = (adapter_factor * joined[:, rank_columns:]).astype(jnp.bfloat16)
    low_spread = got_hot[:, :, None] * lowrank_round[:, None, :]
    grad_spread = got_hot[:, :, None] * gradient_round[:, None, :]

    adapter_output = (
        adapter_factor
        * jnp.einsum("sar,arq->sq", low_spread, adapter_up_weight, preferred_element_type=jnp.float32)
    ).astype(jnp.bfloat16)
    adapter_backward = jnp.einsum(
        "sar,adr->sd", grad_spread, adapter_down_weight, preferred_element_type=jnp.float32
    ).astype(jnp.bfloat16)
    down_grad = jnp.einsum("sd,sar->adr", got_tok, grad_spread, preferred_element_type=jnp.float32)
    up_grad = adapter_factor * jnp.einsum(
        "sar,sq->arq", low_spread, got_cot, preferred_element_type=jnp.float32
    )

    back = jnp.concatenate([adapter_output, adapter_backward], axis=1)
    back, tokens_late = lax.optimization_barrier((back, tokens_full))
    back = lax.all_to_all(back, "dp", split_axis=0, concat_axis=0, tiled=True)
    frozen_output = lax.optimization_barrier(
        jnp.dot(tokens_late, frozen_query_weight, preferred_element_type=jnp.float32)
    )
    mine = jnp.einsum("st,sc->tc", pick, back, preferred_element_type=jnp.float32)
    mine_out = mine[:, :query_portion]
    mine_grad = mine[:, query_portion:]

    projected = (frozen_output + mine_out).astype(jnp.bfloat16)
    input_gradient = (frozen_backward + mine_grad).astype(jnp.bfloat16)
    return (projected, input_gradient, down_grad, up_grad)


def solution(mesh):
    in_specs = (
        P("dp", "tensor"),
        P("dp", "tensor"),
        P(None, "tensor"),
        P("dp", "tensor", None),
        P("dp", None, "tensor"),
        P("dp"),
    )
    out_specs = (
        P("dp", "tensor"),
        P("dp", "tensor"),
        P("dp", "tensor", None),
        P("dp", None, "tensor"),
    )
    return jax.shard_map(
        per_device, mesh=mesh, in_specs=in_specs, out_specs=out_specs, check_vma=False
    )
```

```python
import jax
import jax.numpy as jnp
from jax import lax
from jax.sharding import PartitionSpec as P

adapter_factor = 0.5


def tensor_sum(x, keep_first):
    n = lax.axis_size("tensor")
    half = x.shape[0] // 2
    keep = jnp.where(keep_first, x[:half], x[half:])
    give = jnp.where(keep_first, x[half:], x[:half])
    pair = [(t, t ^ 1) for t in range(n)]
    mine = keep + lax.ppermute(give, "tensor", pair)
    step = 2
    while step < n:
        perm = [(t, t ^ step) for t in range(n)]
        mine = mine + lax.ppermute(mine, "tensor", perm)
        step *= 2
    other = lax.ppermute(mine, "tensor", pair)
    first = jnp.where(keep_first, mine, other)
    second = jnp.where(keep_first, other, mine)
    return jnp.concatenate([first, second], axis=0)


def per_device(
    tokens, cotangent, frozen_query_weight, adapter_down_weight, adapter_up_weight, token_adapter
):
    tok_rows, feature_portion = tokens.shape
    query_portion = cotangent.shape[1]
    local_adapters, _, rank_columns = adapter_down_weight.shape
    dp_size = lax.axis_size("dp")
    capacity = tok_rows // dp_size * 2
    capacity = min(capacity, tok_rows)
    slot_count = dp_size * capacity
    oh_width = 128

    tokens_full = lax.all_gather(tokens, "tensor", axis=1, tiled=True)

    owners = token_adapter // local_adapters
    local_ids = token_adapter % local_adapters
    owner_hits = (owners[:, None] == jnp.arange(dp_size, dtype=jnp.int32)[None, :]).astype(jnp.int32)
    earlier = jnp.cumsum(owner_hits, axis=0) - owner_hits
    rank_in = jnp.sum(earlier * owner_hits, axis=1)
    slot_of = owners * capacity + rank_in
    pick = (jnp.arange(slot_count, dtype=jnp.int32)[:, None] == slot_of[None, :]).astype(jnp.bfloat16)
    local_hot = (local_ids[:, None] == jnp.arange(oh_width, dtype=jnp.int32)[None, :]).astype(
        jnp.bfloat16
    )
    payload = jnp.concatenate([tokens, cotangent, local_hot], axis=1)
    send = jnp.dot(pick, payload, preferred_element_type=jnp.float32).astype(jnp.bfloat16)
    keep_first = lax.axis_index("tensor") % 2 == 0
    send, cot_late, weight_late, keep_first = lax.optimization_barrier(
        (send, cotangent, frozen_query_weight, keep_first)
    )
    partial_term = lax.dot_general(
        cot_late, weight_late, (((1,), (1,)), ((), ())), preferred_element_type=jnp.float32
    )
    frozen_backward = lax.psum_scatter(partial_term, "tensor", scatter_dimension=1, tiled=True)
    got = lax.all_to_all(send, "dp", split_axis=0, concat_axis=0, tiled=True)
    got_tok = got[:, :feature_portion]
    got_cot = got[:, feature_portion : feature_portion + query_portion]
    got_hot = got[:, feature_portion + query_portion : feature_portion + query_portion + local_adapters]
    hot_f = got_hot.astype(jnp.float32)

    hidden_all = jnp.einsum(
        "sd,adr->sar", got_tok, adapter_down_weight, preferred_element_type=jnp.float32
    )
    grad_all = jnp.einsum(
        "sq,arq->sar", got_cot, adapter_up_weight, preferred_element_type=jnp.float32
    )
    hidden_part = jnp.sum(hidden_all * hot_f[:, :, None], axis=1)
    grad_part = jnp.sum(grad_all * hot_f[:, :, None], axis=1)
    joined = tensor_sum(jnp.concatenate([hidden_part, grad_part], axis=1), keep_first)
    lowrank_round = joined[:, :rank_columns].astype(jnp.bfloat16)
    gradient_round = (adapter_factor * joined[:, rank_columns:]).astype(jnp.bfloat16)
    low_spread = got_hot[:, :, None] * lowrank_round[:, None, :]
    grad_spread = got_hot[:, :, None] * gradient_round[:, None, :]

    adapter_output = (
        adapter_factor
        * jnp.einsum("sar,arq->sq", low_spread, adapter_up_weight, preferred_element_type=jnp.float32)
    ).astype(jnp.bfloat16)
    adapter_backward = jnp.einsum(
        "sar,adr->sd", grad_spread, adapter_down_weight, preferred_element_type=jnp.float32
    ).astype(jnp.bfloat16)
    down_grad = jnp.einsum("sd,sar->adr", got_tok, grad_spread, preferred_element_type=jnp.float32)
    up_grad = adapter_factor * jnp.einsum(
        "sar,sq->arq", low_spread, got_cot, preferred_element_type=jnp.float32
    )

    back = jnp.concatenate([adapter_output, adapter_backward], axis=1)
    back, tokens_late = lax.optimization_barrier((back, tokens_full))
    back = lax.all_to_all(back, "dp", split_axis=0, concat_axis=0, tiled=True)
    frozen_output = lax.optimization_barrier(
        jnp.dot(tokens_late, frozen_query_weight, preferred_element_type=jnp.float32)
    )
    mine = jnp.einsum("st,sc->tc", pick, back, preferred_element_type=jnp.float32)
    mine_out = mine[:, :query_portion]
    mine_grad = mine[:, query_portion:]

    projected = (frozen_output + mine_out).astype(jnp.bfloat16)
    input_gradient = (frozen_backward + mine_grad).astype(jnp.bfloat16)
    return (projected, input_gradient, down_grad, up_grad)


def solution(mesh):
    in_specs = (
        P("dp", "tensor"),
        P("dp", "tensor"),
        P(None, "tensor"),
        P("dp", "tensor", None),
        P("dp", None, "tensor"),
        P("dp"),
    )
    out_specs = (
        P("dp", "tensor"),
        P("dp", "tensor"),
        P("dp", "tensor", None),
        P("dp", None, "tensor"),
    )
    return jax.shard_map(
        per_device, mesh=mesh, in_specs=in_specs, out_specs=out_specs, check_vma=False
    )
```

```python
import jax
import jax.numpy as jnp
from jax import lax
from jax.sharding import PartitionSpec as P

adapter_factor = 0.5


def tensor_sum(x, keep_first):
    n = lax.axis_size("tensor")
    half = x.shape[0] // 2
    keep = jnp.where(keep_first, x[:half], x[half:])
    give = jnp.where(keep_first, x[half:], x[:half])
    pair = [(t, t ^ 1) for t in range(n)]
    mine = keep + lax.ppermute(give, "tensor", pair)
    step = 2
    while step < n:
        perm = [(t, t ^ step) for t in range(n)]
        mine = mine + lax.ppermute(mine, "tensor", perm)
        step *= 2
    other = lax.ppermute(mine, "tensor", pair)
    first = jnp.where(keep_first, mine, other)
    second = jnp.where(keep_first, other, mine)
    return jnp.concatenate([first, second], axis=0)


def adapter_low_parts(got, adapter_down_weight, adapter_up_weight, feature_portion, query_portion):
    local_adapters = adapter_down_weight.shape[0]
    got_tok = got[:, :feature_portion]
    got_cot = got[:, feature_portion : feature_portion + query_portion]
    got_hot = got[:, feature_portion + query_portion : feature_portion + query_portion + local_adapters]
    hot_f = got_hot.astype(jnp.float32)
    hidden_all = jnp.einsum(
        "sd,adr->sar", got_tok, adapter_down_weight, preferred_element_type=jnp.float32
    )
    grad_all = jnp.einsum(
        "sq,arq->sar", got_cot, adapter_up_weight, preferred_element_type=jnp.float32
    )
    hidden_part = jnp.sum(hidden_all * hot_f[:, :, None], axis=1)
    grad_part = jnp.sum(grad_all * hot_f[:, :, None], axis=1)
    return jnp.concatenate([hidden_part, grad_part], axis=1)


def adapter_results(got, joined, adapter_down_weight, adapter_up_weight, feature_portion, query_portion):
    local_adapters, _, rank_columns = adapter_down_weight.shape
    got_tok = got[:, :feature_portion]
    got_cot = got[:, feature_portion : feature_portion + query_portion]
    got_hot = got[:, feature_portion + query_portion : feature_portion + query_portion + local_adapters]
    lowrank_round = joined[:, :rank_columns].astype(jnp.bfloat16)
    gradient_round = (adapter_factor * joined[:, rank_columns:]).astype(jnp.bfloat16)
    low_spread = got_hot[:, :, None] * lowrank_round[:, None, :]
    grad_spread = got_hot[:, :, None] * gradient_round[:, None, :]
    adapter_output = (
        adapter_factor
        * jnp.einsum("sar,arq->sq", low_spread, adapter_up_weight, preferred_element_type=jnp.float32)
    ).astype(jnp.bfloat16)
    adapter_backward = jnp.einsum(
        "sar,adr->sd", grad_spread, adapter_down_weight, preferred_element_type=jnp.float32
    ).astype(jnp.bfloat16)
    down_terms = jnp.einsum("sd,sar->adr", got_tok, grad_spread, preferred_element_type=jnp.float32)
    up_terms = jnp.einsum("sar,sq->arq", low_spread, got_cot, preferred_element_type=jnp.float32)
    back = jnp.concatenate([adapter_output, adapter_backward], axis=1)
    return back, down_terms, up_terms


def per_device(
    tokens, cotangent, frozen_query_weight, adapter_down_weight, adapter_up_weight, token_adapter
):
    tok_rows, feature_portion = tokens.shape
    query_portion = cotangent.shape[1]
    local_adapters = adapter_down_weight.shape[0]
    dp_size = lax.axis_size("dp")
    capacity = tok_rows // dp_size * 2
    capacity = min(capacity, tok_rows)
    chunks = 2 if capacity % 16 == 0 else 1
    oh_width = 128
    dims = (adapter_down_weight, adapter_up_weight, feature_portion, query_portion)

    tokens_full = lax.all_gather(tokens, "tensor", axis=1, tiled=True)

    owners = token_adapter // local_adapters
    local_ids = token_adapter % local_adapters
    owner_hits = (owners[:, None] == jnp.arange(dp_size, dtype=jnp.int32)[None, :]).astype(jnp.int32)
    earlier = jnp.cumsum(owner_hits, axis=0) - owner_hits
    rank_in = jnp.sum(earlier * owner_hits, axis=1)
    slot_of = owners * capacity + rank_in
    per_chunk = capacity // chunks
    slot_ids = jnp.arange(dp_size * capacity, dtype=jnp.int32).reshape(dp_size, chunks, per_chunk)
    local_hot = (local_ids[:, None] == jnp.arange(oh_width, dtype=jnp.int32)[None, :]).astype(
        jnp.bfloat16
    )
    payload = jnp.concatenate([tokens, cotangent, local_hot], axis=1)
    picks, sends = [], []
    for c in range(chunks):
        ids = slot_ids[:, c, :].reshape(dp_size * per_chunk)
        pick = (ids[:, None] == slot_of[None, :]).astype(jnp.bfloat16)
        picks.append(pick)
        sends.append(jnp.dot(pick, payload, preferred_element_type=jnp.float32).astype(jnp.bfloat16))
    keep_first = lax.axis_index("tensor") % 2 == 0
    sends, cot_late, weight_late, keep_first = lax.optimization_barrier(
        (sends, cotangent, frozen_query_weight, keep_first)
    )
    partial_term = lax.dot_general(
        cot_late, weight_late, (((1,), (1,)), ((), ())), preferred_element_type=jnp.float32
    )
    frozen_backward = lax.psum_scatter(partial_term, "tensor", scatter_dimension=1, tiled=True)

    gots, lows = [], []
    for c in range(chunks):
        send = sends[c]
        if lows:
            send, lows[-1] = lax.optimization_barrier((send, lows[-1]))
        got = lax.all_to_all(send, "dp", split_axis=0, concat_axis=0, tiled=True)
        gots.append(got)
        lows.append(adapter_low_parts(got, *dims))

    backs, down_grad, up_sum = [], None, None
    for c in range(chunks):
        joined = tensor_sum(lows[c], keep_first)
        back, down_terms, up_terms = adapter_results(gots[c], joined, *dims)
        down_grad = down_terms if down_grad is None else down_grad + down_terms
        up_sum = up_terms if up_sum is None else up_sum + up_terms
        if c == chunks - 1:
            back, tokens_full = lax.optimization_barrier((back, tokens_full))
        backs.append(lax.all_to_all(back, "dp", split_axis=0, concat_axis=0, tiled=True))
    up_grad = adapter_factor * up_sum
    frozen_output = lax.optimization_barrier(
        jnp.dot(tokens_full, frozen_query_weight, preferred_element_type=jnp.float32)
    )
    mine = None
    for c in range(chunks):
        part = jnp.einsum("st,sc->tc", picks[c], backs[c], preferred_element_type=jnp.float32)
        mine = part if mine is None else mine + part
    mine_out = mine[:, :query_portion]
    mine_grad = mine[:, query_portion:]

    projected = (frozen_output + mine_out).astype(jnp.bfloat16)
    input_gradient = (frozen_backward + mine_grad).astype(jnp.bfloat16)
    return (projected, input_gradient, down_grad, up_grad)


def solution(mesh):
    in_specs = (
        P("dp", "tensor"),
        P("dp", "tensor"),
        P(None, "tensor"),
        P("dp", "tensor", None),
        P("dp", None, "tensor"),
        P("dp"),
    )
    out_specs = (
        P("dp", "tensor"),
        P("dp", "tensor"),
        P("dp", "tensor", None),
        P("dp", None, "tensor"),
    )
    return jax.shard_map(
        per_device, mesh=mesh, in_specs=in_specs, out_specs=out_specs, check_vma=False
    )
```

```python
import jax
import jax.numpy as jnp
from jax import lax
from jax.sharding import PartitionSpec as P

adapter_factor = 0.5


def tensor_sum(x, keep_first):
    n = lax.axis_size("tensor")
    half = x.shape[0] // 2
    keep = jnp.where(keep_first, x[:half], x[half:])
    give = jnp.where(keep_first, x[half:], x[:half])
    pair = [(t, t ^ 1) for t in range(n)]
    mine = keep + lax.ppermute(give, "tensor", pair)
    step = 2
    while step < n:
        flip = 2 * step - 2 if step * 2 == n else step
        perm = [(t, t ^ flip) for t in range(n)]
        mine = mine + lax.ppermute(mine, "tensor", perm)
        step *= 2
    other = lax.ppermute(mine, "tensor", pair)
    first = jnp.where(keep_first, mine, other)
    second = jnp.where(keep_first, other, mine)
    return jnp.concatenate([first, second], axis=0)


def per_device(
    tokens, cotangent, frozen_query_weight, adapter_down_weight, adapter_up_weight, token_adapter
):
    tok_rows, feature_portion = tokens.shape
    query_portion = cotangent.shape[1]
    local_adapters, _, rank_columns = adapter_down_weight.shape
    dp_size = lax.axis_size("dp")
    capacity = tok_rows // dp_size * 2
    capacity = min(capacity, tok_rows)
    slot_count = dp_size * capacity
    oh_width = 128

    tokens_full = lax.all_gather(tokens, "tensor", axis=1, tiled=True)

    owners = token_adapter // local_adapters
    local_ids = token_adapter % local_adapters
    owner_hits = (owners[:, None] == jnp.arange(dp_size, dtype=jnp.int32)[None, :]).astype(jnp.int32)
    earlier = jnp.cumsum(owner_hits, axis=0) - owner_hits
    rank_in = jnp.sum(earlier * owner_hits, axis=1)
    slot_of = owners * capacity + rank_in
    pick = (jnp.arange(slot_count, dtype=jnp.int32)[:, None] == slot_of[None, :]).astype(jnp.bfloat16)
    local_hot = (local_ids[:, None] == jnp.arange(oh_width, dtype=jnp.int32)[None, :]).astype(
        jnp.bfloat16
    )
    payload = jnp.concatenate([tokens, cotangent, local_hot], axis=1)
    send = jnp.dot(pick, payload, preferred_element_type=jnp.float32).astype(jnp.bfloat16)
    keep_first = lax.axis_index("tensor") % 2 == 0
    send, cot_late, weight_late, keep_first = lax.optimization_barrier(
        (send, cotangent, frozen_query_weight, keep_first)
    )
    partial_term = lax.dot_general(
        cot_late, weight_late, (((1,), (1,)), ((), ())), preferred_element_type=jnp.float32
    )
    frozen_backward = lax.psum_scatter(partial_term, "tensor", scatter_dimension=1, tiled=True)
    got = lax.all_to_all(send, "dp", split_axis=0, concat_axis=0, tiled=True)
    got_tok = got[:, :feature_portion]
    got_cot = got[:, feature_portion : feature_portion + query_portion]
    got_hot = got[:, feature_portion + query_portion : feature_portion + query_portion + local_adapters]
    hot_f = got_hot.astype(jnp.float32)

    hidden_all = jnp.einsum(
        "sd,adr->sar", got_tok, adapter_down_weight, preferred_element_type=jnp.float32
    )
    grad_all = jnp.einsum(
        "sq,arq->sar", got_cot, adapter_up_weight, preferred_element_type=jnp.float32
    )
    hidden_part = jnp.sum(hidden_all * hot_f[:, :, None], axis=1)
    grad_part = jnp.sum(grad_all * hot_f[:, :, None], axis=1)
    joined = tensor_sum(jnp.concatenate([hidden_part, grad_part], axis=1), keep_first)
    lowrank_round = joined[:, :rank_columns].astype(jnp.bfloat16)
    gradient_round = (adapter_factor * joined[:, rank_columns:]).astype(jnp.bfloat16)
    low_spread = got_hot[:, :, None] * lowrank_round[:, None, :]
    grad_spread = got_hot[:, :, None] * gradient_round[:, None, :]

    adapter_output = (
        adapter_factor
        * jnp.einsum("sar,arq->sq", low_spread, adapter_up_weight, preferred_element_type=jnp.float32)
    ).astype(jnp.bfloat16)
    adapter_backward = jnp.einsum(
        "sar,adr->sd", grad_spread, adapter_down_weight, preferred_element_type=jnp.float32
    ).astype(jnp.bfloat16)
    down_grad = jnp.einsum("sd,sar->adr", got_tok, grad_spread, preferred_element_type=jnp.float32)
    up_grad = adapter_factor * jnp.einsum(
        "sar,sq->arq", low_spread, got_cot, preferred_element_type=jnp.float32
    )

    back = jnp.concatenate([adapter_output, adapter_backward], axis=1)
    back, tokens_late = lax.optimization_barrier((back, tokens_full))
    back = lax.all_to_all(back, "dp", split_axis=0, concat_axis=0, tiled=True)
    frozen_output = lax.optimization_barrier(
        jnp.dot(tokens_late, frozen_query_weight, preferred_element_type=jnp.float32)
    )
    mine_out = jnp.einsum(
        "st,sc->tc", pick, back[:, :query_portion], preferred_element_type=jnp.float32
    )
    mine_grad = jnp.einsum(
        "st,sc->tc", pick, back[:, query_portion:], preferred_element_type=jnp.float32
    )

    projected = (frozen_output + mine_out).astype(jnp.bfloat16)
    input_gradient = (frozen_backward + mine_grad).astype(jnp.bfloat16)
    return (projected, input_gradient, down_grad, up_grad)


def solution(mesh):
    in_specs = (
        P("dp", "tensor"),
        P("dp", "tensor"),
        P(None, "tensor"),
        P("dp", "tensor", None),
        P("dp", None, "tensor"),
        P("dp"),
    )
    out_specs = (
        P("dp", "tensor"),
        P("dp", "tensor"),
        P("dp", "tensor", None),
        P("dp", None, "tensor"),
    )
    return jax.shard_map(
        per_device, mesh=mesh, in_specs=in_specs, out_specs=out_specs, check_vma=False
    )
```

```python
import jax
import jax.numpy as jnp
from jax import lax
from jax.experimental.layout import Layout, with_layout_constraint
from jax.sharding import PartitionSpec as P

adapter_factor = 0.5


def tensor_sum(x, keep_first):
    n = lax.axis_size("tensor")
    half = x.shape[0] // 2
    keep = jnp.where(keep_first, x[:half], x[half:])
    give = jnp.where(keep_first, x[half:], x[:half])
    pair = [(t, t ^ 1) for t in range(n)]
    mine = keep + lax.ppermute(give, "tensor", pair)
    step = 2
    while step < n:
        flip = 2 * step - 2 if step * 2 == n else step
        perm = [(t, t ^ flip) for t in range(n)]
        mine = mine + lax.ppermute(mine, "tensor", perm)
        step *= 2
    other = lax.ppermute(mine, "tensor", pair)
    first = jnp.where(keep_first, mine, other)
    second = jnp.where(keep_first, other, mine)
    return jnp.concatenate([first, second], axis=0)


def per_device(
    tokens, cotangent, frozen_query_weight, adapter_down_weight, adapter_up_weight, token_adapter
):
    tok_rows, feature_portion = tokens.shape
    query_portion = cotangent.shape[1]
    local_adapters, _, rank_columns = adapter_down_weight.shape
    dp_size = lax.axis_size("dp")
    capacity = tok_rows // dp_size * 2
    capacity = min(capacity, tok_rows)
    slot_count = dp_size * capacity
    oh_width = 128

    tokens_full = lax.all_gather(tokens, "tensor", axis=1, tiled=True)

    owners = token_adapter // local_adapters
    local_ids = token_adapter % local_adapters
    owner_hits = (owners[:, None] == jnp.arange(dp_size, dtype=jnp.int32)[None, :]).astype(jnp.int32)
    earlier = jnp.cumsum(owner_hits, axis=0) - owner_hits
    rank_in = jnp.sum(earlier * owner_hits, axis=1)
    slot_of = owners * capacity + rank_in
    pick = (jnp.arange(slot_count, dtype=jnp.int32)[:, None] == slot_of[None, :]).astype(jnp.bfloat16)
    local_hot = (local_ids[:, None] == jnp.arange(oh_width, dtype=jnp.int32)[None, :]).astype(
        jnp.bfloat16
    )
    payload = jnp.concatenate([tokens, cotangent, local_hot], axis=1)
    send = jnp.dot(pick, payload, preferred_element_type=jnp.float32).astype(jnp.bfloat16)
    keep_first = lax.axis_index("tensor") % 2 == 0
    send, cot_late, weight_late, keep_first = lax.optimization_barrier(
        (send, cotangent, frozen_query_weight, keep_first)
    )
    partial_term = lax.dot_general(
        cot_late, weight_late, (((1,), (1,)), ((), ())), preferred_element_type=jnp.float32
    )
    frozen_backward = lax.psum_scatter(partial_term, "tensor", scatter_dimension=1, tiled=True)
    got = lax.all_to_all(send, "dp", split_axis=0, concat_axis=0, tiled=True)
    got_tok = got[:, :feature_portion]
    got_cot = got[:, feature_portion : feature_portion + query_portion]
    got_hot = got[:, feature_portion + query_portion : feature_portion + query_portion + local_adapters]
    hot_f = got_hot.astype(jnp.float32)

    hidden_all = jnp.einsum(
        "sd,adr->sar", got_tok, adapter_down_weight, preferred_element_type=jnp.float32
    )
    grad_all = jnp.einsum(
        "sq,arq->sar", got_cot, adapter_up_weight, preferred_element_type=jnp.float32
    )
    hidden_part = jnp.sum(hidden_all * hot_f[:, :, None], axis=1)
    grad_part = jnp.sum(grad_all * hot_f[:, :, None], axis=1)
    joined = tensor_sum(jnp.concatenate([hidden_part, grad_part], axis=1), keep_first)
    lowrank_round = joined[:, :rank_columns].astype(jnp.bfloat16)
    gradient_round = (adapter_factor * joined[:, rank_columns:]).astype(jnp.bfloat16)
    low_spread = got_hot[:, :, None] * lowrank_round[:, None, :]
    grad_spread = got_hot[:, :, None] * gradient_round[:, None, :]

    adapter_output = (
        adapter_factor
        * jnp.einsum("sar,arq->sq", low_spread, adapter_up_weight, preferred_element_type=jnp.float32)
    ).astype(jnp.bfloat16)
    adapter_backward = jnp.einsum(
        "sar,adr->sd", grad_spread, adapter_down_weight, preferred_element_type=jnp.float32
    ).astype(jnp.bfloat16)
    down_grad = jnp.einsum("sd,sar->adr", got_tok, grad_spread, preferred_element_type=jnp.float32)
    up_grad = adapter_factor * jnp.einsum(
        "sar,sq->arq", low_spread, got_cot, preferred_element_type=jnp.float32
    )

    adapter_output = with_layout_constraint(adapter_output, Layout(major_to_minor=(0, 1)))
    adapter_backward = with_layout_constraint(adapter_backward, Layout(major_to_minor=(0, 1)))
    back = jnp.concatenate([adapter_output, adapter_backward], axis=1)
    back, tokens_late = lax.optimization_barrier((back, tokens_full))
    back = lax.all_to_all(back, "dp", split_axis=0, concat_axis=0, tiled=True)
    frozen_output = lax.optimization_barrier(
        jnp.dot(tokens_late, frozen_query_weight, preferred_element_type=jnp.float32)
    )
    mine_out = jnp.einsum(
        "st,sc->tc", pick, back[:, :query_portion], preferred_element_type=jnp.float32
    )
    mine_grad = jnp.einsum(
        "st,sc->tc", pick, back[:, query_portion:], preferred_element_type=jnp.float32
    )

    projected = (frozen_output + mine_out).astype(jnp.bfloat16)
    input_gradient = (frozen_backward + mine_grad).astype(jnp.bfloat16)
    return (projected, input_gradient, down_grad, up_grad)


def solution(mesh):
    in_specs = (
        P("dp", "tensor"),
        P("dp", "tensor"),
        P(None, "tensor"),
        P("dp", "tensor", None),
        P("dp", None, "tensor"),
        P("dp"),
    )
    out_specs = (
        P("dp", "tensor"),
        P("dp", "tensor"),
        P("dp", "tensor", None),
        P("dp", None, "tensor"),
    )
    return jax.shard_map(
        per_device, mesh=mesh, in_specs=in_specs, out_specs=out_specs, check_vma=False
    )
```

```python
import jax
import jax.numpy as jnp
from jax import lax
from jax.experimental.layout import Layout, with_layout_constraint
from jax.sharding import PartitionSpec as P

adapter_factor = 0.5


def tensor_sum(x, keep_first):
    n = lax.axis_size("tensor")
    half = x.shape[0] // 2
    keep = jnp.where(keep_first, x[:half], x[half:])
    give = jnp.where(keep_first, x[half:], x[:half])
    pair = [(t, t ^ 1) for t in range(n)]
    mine = keep + lax.ppermute(give, "tensor", pair)
    step = 2
    while step < n:
        flip = 2 * step - 2 if step * 2 == n else step
        perm = [(t, t ^ flip) for t in range(n)]
        mine = mine + lax.ppermute(mine, "tensor", perm)
        step *= 2
    other = lax.ppermute(mine, "tensor", pair)
    first = jnp.where(keep_first, mine, other)
    second = jnp.where(keep_first, other, mine)
    return jnp.concatenate([first, second], axis=0)


def per_device(
    tokens, cotangent, frozen_query_weight, adapter_down_weight, adapter_up_weight, token_adapter
):
    tok_rows, feature_portion = tokens.shape
    query_portion = cotangent.shape[1]
    local_adapters, _, rank_columns = adapter_down_weight.shape
    dp_size = lax.axis_size("dp")
    capacity = tok_rows // dp_size * 2
    capacity = min(capacity, tok_rows)
    slot_count = dp_size * capacity
    oh_width = 128

    tokens_full = lax.all_gather(tokens, "tensor", axis=1, tiled=True)

    owners = token_adapter // local_adapters
    local_ids = token_adapter % local_adapters
    owner_hits = (owners[:, None] == jnp.arange(dp_size, dtype=jnp.int32)[None, :]).astype(jnp.int32)
    earlier = jnp.cumsum(owner_hits, axis=0) - owner_hits
    rank_in = jnp.sum(earlier * owner_hits, axis=1)
    slot_of = owners * capacity + rank_in
    pick = (jnp.arange(slot_count, dtype=jnp.int32)[:, None] == slot_of[None, :]).astype(jnp.bfloat16)
    local_hot = (local_ids[:, None] == jnp.arange(oh_width, dtype=jnp.int32)[None, :]).astype(
        jnp.bfloat16
    )
    payload = jnp.concatenate([tokens, cotangent, local_hot], axis=1)
    send = jnp.dot(pick, payload, preferred_element_type=jnp.float32).astype(jnp.bfloat16)
    keep_first = lax.axis_index("tensor") % 2 == 0
    send, cot_late, weight_late, keep_first = lax.optimization_barrier(
        (send, cotangent, frozen_query_weight, keep_first)
    )
    partial_term = lax.dot_general(
        cot_late, weight_late, (((1,), (1,)), ((), ())), preferred_element_type=jnp.float32
    )
    frozen_backward = lax.psum_scatter(partial_term, "tensor", scatter_dimension=1, tiled=True)
    got = lax.all_to_all(send, "dp", split_axis=0, concat_axis=0, tiled=True)
    got_tok = got[:, :feature_portion]
    got_cot = got[:, feature_portion : feature_portion + query_portion]
    got_hot = got[:, feature_portion + query_portion : feature_portion + query_portion + local_adapters]
    hot_f = got_hot.astype(jnp.float32)

    hidden_all = jnp.einsum(
        "sd,adr->sar", got_tok, adapter_down_weight, preferred_element_type=jnp.float32
    )
    grad_all = jnp.einsum(
        "sq,arq->sar", got_cot, adapter_up_weight, preferred_element_type=jnp.float32
    )
    hidden_part = jnp.sum(hidden_all * hot_f[:, :, None], axis=1)
    grad_part = jnp.sum(grad_all * hot_f[:, :, None], axis=1)
    joined = tensor_sum(jnp.concatenate([hidden_part, grad_part], axis=1), keep_first)
    lowrank_round = joined[:, :rank_columns].astype(jnp.bfloat16)
    gradient_round = (adapter_factor * joined[:, rank_columns:]).astype(jnp.bfloat16)
    low_spread = got_hot[:, :, None] * lowrank_round[:, None, :]
    grad_spread = got_hot[:, :, None] * gradient_round[:, None, :]

    adapter_output = (
        adapter_factor
        * jnp.einsum("sar,arq->sq", low_spread, adapter_up_weight, preferred_element_type=jnp.float32)
    ).astype(jnp.bfloat16)
    adapter_backward = jnp.einsum(
        "sar,adr->sd", grad_spread, adapter_down_weight, preferred_element_type=jnp.float32
    ).astype(jnp.bfloat16)
    down_grad = jnp.einsum("sd,sar->adr", got_tok, grad_spread, preferred_element_type=jnp.float32)
    up_grad = adapter_factor * jnp.einsum(
        "sar,sq->arq", low_spread, got_cot, preferred_element_type=jnp.float32
    )

    adapter_output = with_layout_constraint(adapter_output, Layout(major_to_minor=(0, 1)))
    adapter_backward = with_layout_constraint(adapter_backward, Layout(major_to_minor=(0, 1)))
    back = jnp.concatenate([adapter_output, adapter_backward], axis=1)
    back, tokens_late = lax.optimization_barrier((back, tokens_full))
    back = lax.all_to_all(back, "dp", split_axis=0, concat_axis=0, tiled=True)
    frozen_output = lax.optimization_barrier(
        jnp.dot(tokens_late, frozen_query_weight, preferred_element_type=jnp.float32)
    )
    pick_rows = (slot_of[:, None] == jnp.arange(slot_count, dtype=jnp.int32)[None, :]).astype(
        jnp.bfloat16
    )
    mine_out = jnp.dot(pick_rows, back[:, :query_portion], preferred_element_type=jnp.float32)
    mine_grad = jnp.dot(pick_rows, back[:, query_portion:], preferred_element_type=jnp.float32)

    projected = (frozen_output + mine_out).astype(jnp.bfloat16)
    input_gradient = (frozen_backward + mine_grad).astype(jnp.bfloat16)
    return (projected, input_gradient, down_grad, up_grad)


def solution(mesh):
    in_specs = (
        P("dp", "tensor"),
        P("dp", "tensor"),
        P(None, "tensor"),
        P("dp", "tensor", None),
        P("dp", None, "tensor"),
        P("dp"),
    )
    out_specs = (
        P("dp", "tensor"),
        P("dp", "tensor"),
        P("dp", "tensor", None),
        P("dp", None, "tensor"),
    )
    return jax.shard_map(
        per_device, mesh=mesh, in_specs=in_specs, out_specs=out_specs, check_vma=False
    )
```

```python
import jax
import jax.numpy as jnp
from jax import lax
from jax.experimental.layout import Layout, with_layout_constraint
from jax.sharding import PartitionSpec as P

adapter_factor = 0.5


def tensor_sum(x, keep_first):
    n = lax.axis_size("tensor")
    half = x.shape[0] // 2
    keep = jnp.where(keep_first, x[:half], x[half:])
    give = jnp.where(keep_first, x[half:], x[:half])
    pair = [(t, t ^ 1) for t in range(n)]
    mine = keep + lax.ppermute(give, "tensor", pair)
    step = 2
    while step < n:
        flip = 2 * step - 2 if step * 2 == n else step
        perm = [(t, t ^ flip) for t in range(n)]
        mine = mine + lax.ppermute(mine, "tensor", perm)
        step *= 2
    other = lax.ppermute(mine, "tensor", pair)
    first = jnp.where(keep_first, mine, other)
    second = jnp.where(keep_first, other, mine)
    return jnp.concatenate([first, second], axis=0)


def per_device(
    tokens, cotangent, frozen_query_weight, adapter_down_weight, adapter_up_weight, token_adapter
):
    tok_rows, feature_portion = tokens.shape
    query_portion = cotangent.shape[1]
    local_adapters, _, rank_columns = adapter_down_weight.shape
    dp_size = lax.axis_size("dp")
    capacity = tok_rows // dp_size * 2
    capacity = min(capacity, tok_rows)
    slot_count = dp_size * capacity
    oh_width = 128

    tokens_full = lax.all_gather(tokens, "tensor", axis=1, tiled=True)

    owners = token_adapter // local_adapters
    local_ids = token_adapter % local_adapters
    owner_hits = (owners[:, None] == jnp.arange(dp_size, dtype=jnp.int32)[None, :]).astype(jnp.int32)
    earlier = jnp.cumsum(owner_hits, axis=0) - owner_hits
    rank_in = jnp.sum(earlier * owner_hits, axis=1)
    slot_of = owners * capacity + rank_in
    pick = (jnp.arange(slot_count, dtype=jnp.int32)[:, None] == slot_of[None, :]).astype(jnp.bfloat16)
    local_hot = (local_ids[:, None] == jnp.arange(oh_width, dtype=jnp.int32)[None, :]).astype(
        jnp.bfloat16
    )
    send = jnp.concatenate(
        [
            with_layout_constraint(
                jnp.dot(pick, part, preferred_element_type=jnp.float32).astype(jnp.bfloat16),
                Layout(major_to_minor=(0, 1)),
            )
            for part in (tokens, cotangent, local_hot)
        ],
        axis=1,
    )
    keep_first = lax.axis_index("tensor") % 2 == 0
    send, cot_late, weight_late, keep_first = lax.optimization_barrier(
        (send, cotangent, frozen_query_weight, keep_first)
    )
    partial_term = lax.dot_general(
        cot_late, weight_late, (((1,), (1,)), ((), ())), preferred_element_type=jnp.float32
    )
    frozen_backward = lax.psum_scatter(partial_term, "tensor", scatter_dimension=1, tiled=True)
    got = lax.all_to_all(send, "dp", split_axis=0, concat_axis=0, tiled=True)
    got_tok = got[:, :feature_portion]
    got_cot = got[:, feature_portion : feature_portion + query_portion]
    got_hot = got[:, feature_portion + query_portion : feature_portion + query_portion + local_adapters]
    hot_f = got_hot.astype(jnp.float32)

    hidden_all = jnp.einsum(
        "sd,adr->sar", got_tok, adapter_down_weight, preferred_element_type=jnp.float32
    )
    grad_all = jnp.einsum(
        "sq,arq->sar", got_cot, adapter_up_weight, preferred_element_type=jnp.float32
    )
    hidden_part = jnp.sum(hidden_all * hot_f[:, :, None], axis=1)
    grad_part = jnp.sum(grad_all * hot_f[:, :, None], axis=1)
    joined = tensor_sum(jnp.concatenate([hidden_part, grad_part], axis=1), keep_first)
    lowrank_round = joined[:, :rank_columns].astype(jnp.bfloat16)
    gradient_round = (adapter_factor * joined[:, rank_columns:]).astype(jnp.bfloat16)
    low_spread = got_hot[:, :, None] * lowrank_round[:, None, :]
    grad_spread = got_hot[:, :, None] * gradient_round[:, None, :]

    adapter_output = (
        adapter_factor
        * jnp.einsum("sar,arq->sq", low_spread, adapter_up_weight, preferred_element_type=jnp.float32)
    ).astype(jnp.bfloat16)
    adapter_backward = jnp.einsum(
        "sar,adr->sd", grad_spread, adapter_down_weight, preferred_element_type=jnp.float32
    ).astype(jnp.bfloat16)
    down_grad = jnp.einsum("sd,sar->adr", got_tok, grad_spread, preferred_element_type=jnp.float32)
    up_grad = adapter_factor * jnp.einsum(
        "sar,sq->arq", low_spread, got_cot, preferred_element_type=jnp.float32
    )

    adapter_output = with_layout_constraint(adapter_output, Layout(major_to_minor=(0, 1)))
    adapter_backward = with_layout_constraint(adapter_backward, Layout(major_to_minor=(0, 1)))
    back = jnp.concatenate([adapter_output, adapter_backward], axis=1)
    back, tokens_late = lax.optimization_barrier((back, tokens_full))
    back = lax.all_to_all(back, "dp", split_axis=0, concat_axis=0, tiled=True)
    frozen_output = lax.optimization_barrier(
        jnp.dot(tokens_late, frozen_query_weight, preferred_element_type=jnp.float32)
    )
    mine_out = jnp.einsum(
        "st,sc->tc", pick, back[:, :query_portion], preferred_element_type=jnp.float32
    )
    mine_grad = jnp.einsum(
        "st,sc->tc", pick, back[:, query_portion:], preferred_element_type=jnp.float32
    )

    projected = (frozen_output + mine_out).astype(jnp.bfloat16)
    input_gradient = (frozen_backward + mine_grad).astype(jnp.bfloat16)
    return (projected, input_gradient, down_grad, up_grad)


def solution(mesh):
    in_specs = (
        P("dp", "tensor"),
        P("dp", "tensor"),
        P(None, "tensor"),
        P("dp", "tensor", None),
        P("dp", None, "tensor"),
        P("dp"),
    )
    out_specs = (
        P("dp", "tensor"),
        P("dp", "tensor"),
        P("dp", "tensor", None),
        P("dp", None, "tensor"),
    )
    return jax.shard_map(
        per_device, mesh=mesh, in_specs=in_specs, out_specs=out_specs, check_vma=False
    )
```

```python
import jax
import jax.numpy as jnp
from jax import lax
from jax.experimental.layout import Layout, with_layout_constraint
from jax.sharding import PartitionSpec as P

adapter_factor = 0.5


def tensor_sum(x, keep_first):
    n = lax.axis_size("tensor")
    half = x.shape[0] // 2
    keep = jnp.where(keep_first, x[:half], x[half:])
    give = jnp.where(keep_first, x[half:], x[:half])
    pair = [(t, t ^ 1) for t in range(n)]
    mine = keep + lax.ppermute(give, "tensor", pair)
    if n == 8:
        got = [lax.ppermute(mine, "tensor", [(t, t ^ f) for t in range(n)]) for f in (2, 4, 6)]
        mine = (mine + got[0]) + (got[1] + got[2])
    else:
        step = 2
        while step < n:
            perm = [(t, t ^ step) for t in range(n)]
            mine = mine + lax.ppermute(mine, "tensor", perm)
            step *= 2
    other = lax.ppermute(mine, "tensor", pair)
    first = jnp.where(keep_first, mine, other)
    second = jnp.where(keep_first, other, mine)
    return jnp.concatenate([first, second], axis=0)


def per_device(
    tokens, cotangent, frozen_query_weight, adapter_down_weight, adapter_up_weight, token_adapter
):
    tok_rows, feature_portion = tokens.shape
    query_portion = cotangent.shape[1]
    local_adapters, _, rank_columns = adapter_down_weight.shape
    dp_size = lax.axis_size("dp")
    capacity = tok_rows // dp_size * 2
    capacity = min(capacity, tok_rows)
    slot_count = dp_size * capacity
    oh_width = 128

    tokens_full = lax.all_gather(tokens, "tensor", axis=1, tiled=True)

    owners = token_adapter // local_adapters
    local_ids = token_adapter % local_adapters
    owner_hits = (owners[:, None] == jnp.arange(dp_size, dtype=jnp.int32)[None, :]).astype(jnp.int32)
    earlier = jnp.cumsum(owner_hits, axis=0) - owner_hits
    rank_in = jnp.sum(earlier * owner_hits, axis=1)
    slot_of = owners * capacity + rank_in
    pick = (jnp.arange(slot_count, dtype=jnp.int32)[:, None] == slot_of[None, :]).astype(jnp.bfloat16)
    local_hot = (local_ids[:, None] == jnp.arange(oh_width, dtype=jnp.int32)[None, :]).astype(
        jnp.bfloat16
    )
    payload = jnp.concatenate([tokens, cotangent, local_hot], axis=1)
    send = jnp.dot(pick, payload, preferred_element_type=jnp.float32).astype(jnp.bfloat16)
    keep_first = lax.axis_index("tensor") % 2 == 0
    send, cot_late, weight_late, keep_first = lax.optimization_barrier(
        (send, cotangent, frozen_query_weight, keep_first)
    )
    partial_term = lax.dot_general(
        cot_late, weight_late, (((1,), (1,)), ((), ())), preferred_element_type=jnp.float32
    )
    frozen_backward = lax.psum_scatter(partial_term, "tensor", scatter_dimension=1, tiled=True)
    got = lax.all_to_all(send, "dp", split_axis=0, concat_axis=0, tiled=True)
    got_tok = got[:, :feature_portion]
    got_cot = got[:, feature_portion : feature_portion + query_portion]
    got_hot = got[:, feature_portion + query_portion : feature_portion + query_portion + local_adapters]
    hot_f = got_hot.astype(jnp.float32)

    hidden_all = jnp.einsum(
        "sd,adr->sar", got_tok, adapter_down_weight, preferred_element_type=jnp.float32
    )
    grad_all = jnp.einsum(
        "sq,arq->sar", got_cot, adapter_up_weight, preferred_element_type=jnp.float32
    )
    hidden_part = jnp.sum(hidden_all * hot_f[:, :, None], axis=1)
    grad_part = jnp.sum(grad_all * hot_f[:, :, None], axis=1)
    joined = tensor_sum(jnp.concatenate([hidden_part, grad_part], axis=1), keep_first)
    lowrank_round = joined[:, :rank_columns].astype(jnp.bfloat16)
    gradient_round = (adapter_factor * joined[:, rank_columns:]).astype(jnp.bfloat16)
    low_spread = got_hot[:, :, None] * lowrank_round[:, None, :]
    grad_spread = got_hot[:, :, None] * gradient_round[:, None, :]

    adapter_output = (
        adapter_factor
        * jnp.einsum("sar,arq->sq", low_spread, adapter_up_weight, preferred_element_type=jnp.float32)
    ).astype(jnp.bfloat16)
    adapter_backward = jnp.einsum(
        "sar,adr->sd", grad_spread, adapter_down_weight, preferred_element_type=jnp.float32
    ).astype(jnp.bfloat16)
    down_grad = jnp.einsum("sd,sar->adr", got_tok, grad_spread, preferred_element_type=jnp.float32)
    up_grad = adapter_factor * jnp.einsum(
        "sar,sq->arq", low_spread, got_cot, preferred_element_type=jnp.float32
    )

    adapter_output = with_layout_constraint(adapter_output, Layout(major_to_minor=(0, 1)))
    adapter_backward = with_layout_constraint(adapter_backward, Layout(major_to_minor=(0, 1)))
    back = jnp.concatenate([adapter_output, adapter_backward], axis=1)
    back, tokens_late = lax.optimization_barrier((back, tokens_full))
    back = lax.all_to_all(back, "dp", split_axis=0, concat_axis=0, tiled=True)
    frozen_output = lax.optimization_barrier(
        jnp.dot(tokens_late, frozen_query_weight, preferred_element_type=jnp.float32)
    )
    mine_out = jnp.einsum(
        "st,sc->tc", pick, back[:, :query_portion], preferred_element_type=jnp.float32
    )
    mine_grad = jnp.einsum(
        "st,sc->tc", pick, back[:, query_portion:], preferred_element_type=jnp.float32
    )

    projected = (frozen_output + mine_out).astype(jnp.bfloat16)
    input_gradient = (frozen_backward + mine_grad).astype(jnp.bfloat16)
    return (projected, input_gradient, down_grad, up_grad)


def solution(mesh):
    in_specs = (
        P("dp", "tensor"),
        P("dp", "tensor"),
        P(None, "tensor"),
        P("dp", "tensor", None),
        P("dp", None, "tensor"),
        P("dp"),
    )
    out_specs = (
        P("dp", "tensor"),
        P("dp", "tensor"),
        P("dp", "tensor", None),
        P("dp", None, "tensor"),
    )
    return jax.shard_map(
        per_device, mesh=mesh, in_specs=in_specs, out_specs=out_specs, check_vma=False
    )
```

```python
import jax
import jax.numpy as jnp
from jax import lax
from jax.experimental.layout import Layout, with_layout_constraint
from jax.sharding import PartitionSpec as P

adapter_factor = 0.5


def tensor_sum(x, keep_first):
    n = lax.axis_size("tensor")
    half = x.shape[0] // 2
    keep = jnp.where(keep_first, x[:half], x[half:])
    give = jnp.where(keep_first, x[half:], x[:half])
    pair = [(t, t ^ 1) for t in range(n)]
    mine = keep + lax.ppermute(give, "tensor", pair)
    if n == 8:
        got = [lax.ppermute(mine, "tensor", [(t, t ^ f) for t in range(n)]) for f in (2, 6)]
        far = [(t, t ^ 4) for t in range(n)]
        quarter = mine.shape[0] // 2
        got.insert(1, jnp.concatenate(
            [lax.ppermute(mine[:quarter], "tensor", far), lax.ppermute(mine[quarter:], "tensor", far)],
            axis=0,
        ))
        mine = (mine + got[0]) + (got[1] + got[2])
    else:
        step = 2
        while step < n:
            perm = [(t, t ^ step) for t in range(n)]
            mine = mine + lax.ppermute(mine, "tensor", perm)
            step *= 2
    other = lax.ppermute(mine, "tensor", pair)
    first = jnp.where(keep_first, mine, other)
    second = jnp.where(keep_first, other, mine)
    return jnp.concatenate([first, second], axis=0)


def per_device(
    tokens, cotangent, frozen_query_weight, adapter_down_weight, adapter_up_weight, token_adapter
):
    tok_rows, feature_portion = tokens.shape
    query_portion = cotangent.shape[1]
    local_adapters, _, rank_columns = adapter_down_weight.shape
    dp_size = lax.axis_size("dp")
    capacity = tok_rows // dp_size * 2
    capacity = min(capacity, tok_rows)
    slot_count = dp_size * capacity
    oh_width = 128

    tokens_full = lax.all_gather(tokens, "tensor", axis=1, tiled=True)

    owners = token_adapter // local_adapters
    local_ids = token_adapter % local_adapters
    owner_hits = (owners[:, None] == jnp.arange(dp_size, dtype=jnp.int32)[None, :]).astype(jnp.int32)
    earlier = jnp.cumsum(owner_hits, axis=0) - owner_hits
    rank_in = jnp.sum(earlier * owner_hits, axis=1)
    slot_of = owners * capacity + rank_in
    pick = (jnp.arange(slot_count, dtype=jnp.int32)[:, None] == slot_of[None, :]).astype(jnp.bfloat16)
    local_hot = (local_ids[:, None] == jnp.arange(oh_width, dtype=jnp.int32)[None, :]).astype(
        jnp.bfloat16
    )
    payload = jnp.concatenate([tokens, cotangent, local_hot], axis=1)
    send = jnp.dot(pick, payload, preferred_element_type=jnp.float32).astype(jnp.bfloat16)
    keep_first = lax.axis_index("tensor") % 2 == 0
    send, cot_late, weight_late, keep_first = lax.optimization_barrier(
        (send, cotangent, frozen_query_weight, keep_first)
    )
    partial_term = lax.dot_general(
        cot_late, weight_late, (((1,), (1,)), ((), ())), preferred_element_type=jnp.float32
    )
    frozen_backward = lax.psum_scatter(partial_term, "tensor", scatter_dimension=1, tiled=True)
    got = lax.all_to_all(send, "dp", split_axis=0, concat_axis=0, tiled=True)
    got_tok = got[:, :feature_portion]
    got_cot = got[:, feature_portion : feature_portion + query_portion]
    got_hot = got[:, feature_portion + query_portion : feature_portion + query_portion + local_adapters]
    hot_f = got_hot.astype(jnp.float32)

    hidden_all = jnp.einsum(
        "sd,adr->sar", got_tok, adapter_down_weight, preferred_element_type=jnp.float32
    )
    grad_all = jnp.einsum(
        "sq,arq->sar", got_cot, adapter_up_weight, preferred_element_type=jnp.float32
    )
    hidden_part = jnp.sum(hidden_all * hot_f[:, :, None], axis=1)
    grad_part = jnp.sum(grad_all * hot_f[:, :, None], axis=1)
    joined = tensor_sum(jnp.concatenate([hidden_part, grad_part], axis=1), keep_first)
    lowrank_round = joined[:, :rank_columns].astype(jnp.bfloat16)
    gradient_round = (adapter_factor * joined[:, rank_columns:]).astype(jnp.bfloat16)
    low_spread = got_hot[:, :, None] * lowrank_round[:, None, :]
    grad_spread = got_hot[:, :, None] * gradient_round[:, None, :]

    adapter_output = (
        adapter_factor
        * jnp.einsum("sar,arq->sq", low_spread, adapter_up_weight, preferred_element_type=jnp.float32)
    ).astype(jnp.bfloat16)
    adapter_backward = jnp.einsum(
        "sar,adr->sd", grad_spread, adapter_down_weight, preferred_element_type=jnp.float32
    ).astype(jnp.bfloat16)
    down_grad = jnp.einsum("sd,sar->adr", got_tok, grad_spread, preferred_element_type=jnp.float32)
    up_grad = adapter_factor * jnp.einsum(
        "sar,sq->arq", low_spread, got_cot, preferred_element_type=jnp.float32
    )

    adapter_output = with_layout_constraint(adapter_output, Layout(major_to_minor=(0, 1)))
    adapter_backward = with_layout_constraint(adapter_backward, Layout(major_to_minor=(0, 1)))
    back = jnp.concatenate([adapter_output, adapter_backward], axis=1)
    back, tokens_late = lax.optimization_barrier((back, tokens_full))
    back = lax.all_to_all(back, "dp", split_axis=0, concat_axis=0, tiled=True)
    frozen_output = lax.optimization_barrier(
        jnp.dot(tokens_late, frozen_query_weight, preferred_element_type=jnp.float32)
    )
    mine_out = jnp.einsum(
        "st,sc->tc", pick, back[:, :query_portion], preferred_element_type=jnp.float32
    )
    mine_grad = jnp.einsum(
        "st,sc->tc", pick, back[:, query_portion:], preferred_element_type=jnp.float32
    )

    projected = (frozen_output + mine_out).astype(jnp.bfloat16)
    input_gradient = (frozen_backward + mine_grad).astype(jnp.bfloat16)
    return (projected, input_gradient, down_grad, up_grad)


def solution(mesh):
    in_specs = (
        P("dp", "tensor"),
        P("dp", "tensor"),
        P(None, "tensor"),
        P("dp", "tensor", None),
        P("dp", None, "tensor"),
        P("dp"),
    )
    out_specs = (
        P("dp", "tensor"),
        P("dp", "tensor"),
        P("dp", "tensor", None),
        P("dp", None, "tensor"),
    )
    return jax.shard_map(
        per_device, mesh=mesh, in_specs=in_specs, out_specs=out_specs, check_vma=False
    )
```
